256 devices in a mesh: chan: 64 (over z, y_lo, x), ma: 4 (over y_hi, core).
Axes of the slice: x: 4, y: 4 (y_hi: 2, y_lo: 2; y = y_hi * 2 + y_lo), z: 8, core: 2. Of those that a mesh axis runs over, the one named last changes fastest.
Arguments:
- beam_table: bfloat16 [512, 1024, 2048], P(('ma', 'chan')), parts along dimension 0, may hold values from -0.125 to 0.125
- covariance: bfloat16 [8192, 128, 128], P(('ma', 'chan')), parts along dimension 0, as said below
- noise_var: float32 [512, 512], P(('ma', 'chan')), parts along dimension 0, may hold values from 0.5 to 4
- start_field: float32 [512, 512, 256], P(('ma', 'chan')), parts along dimension 0, may hold values from -4 to 4
- probes: float32 [512, 512, 256], P(('ma', 'chan')), parts along dimension 0, may hold values from -6 to 6
Outputs:
- solved: float32 [512, 512, 256], P(('ma', 'chan')), parts along dimension 0
- multipole_band_power: bfloat16 [8192, 128, 128], P(('ma', 'chan')), parts along dimension 0
The draws below stay inside these ranges and needn't reach their ends.
There are 4 independent parts, one for each index of `ma`. The reference program is written for one: setup_inputs(seed, part) draws one part's arguments, and reference() takes and returns one part's arrays. A program takes and returns all parts, laid end to end along the dimension named above; each array names one. Nothing has to cross between parts.
Inputs may be any that keep to these rules, and one draw needn't show every extreme that they name: Each covariance[l] is symmetric with diagonal entries between 1 and 2.
All inputs are finite; a program needn't handle non-finite values.
Results may differ from the reference program's by a relative error of at most 0.009.
Values may be sent and summed in bfloat16 or wider, within the bound.
No kernel may reach another device: no remote copies, remote signals or barrier semaphores. Data moves between devices by JAX's collectives and lax.ppermute only.
A program may use at most 128 MiB of HBM per device.

```python
import math
import jax
import jax.numpy as jnp
from jax import lax

CHANNELS = 128
K = 512
L = 2048
PROBE_VECTOR_COUNT = 128
ITERS = 2


def draw_covariance(key, part):
    first_key = jax.random.fold_in(key, 11)
    second_key = jax.random.fold_in(key, 12)
    raw_values = jax.random.uniform(first_key, (L, CHANNELS, CHANNELS), jnp.float32, -1.0, 1.0)
    symmetric = 0.5 * (raw_values + jnp.swapaxes(raw_values, 1, 2))
    identity = jnp.eye(CHANNELS, dtype=jnp.float32)
    diagonal = 1.0 + jax.random.uniform(second_key, (L, CHANNELS, 1), jnp.float32)
    offdiag = (1.0 - identity) * (0.9 / math.sqrt(CHANNELS)) * symmetric
    return (identity * diagonal + offdiag).astype(jnp.bfloat16)


def block_scale(own_key, dims, split, smallest, largest):
    loudness, own = 1.0, jax.random.fold_in(own_key, 6)
    for position, parts in split:
        steps = jnp.exp(jax.random.uniform(jax.random.fold_in(own, position), (parts,), jnp.float32, smallest / len(split), largest / len(split)))
        loudness = loudness * jnp.repeat(steps, dims[position] // parts).reshape([-1 if axis == position else 1 for axis in range(len(dims))])
    return loudness


def scatter_about(own_key, dims, scale, bound, split=(), kind=jnp.bfloat16):
    values = jax.random.normal(own_key, dims, jnp.float32) * scale
    if len(split) > 0:
        values = block_scale(own_key, dims, split, -0.22, 0.18) * values
    return jnp.clip(values, min=-bound, max=bound).astype(kind)


def setup_inputs(seed: int = 0, part: int = 0) -> dict:
    streams_of = jax.random.split(jax.random.key(seed), 6)
    part_keys = jax.random.split(jax.random.fold_in(streams_of[5], part), 6)
    beam_table = scatter_about(part_keys[0], (CHANNELS, 2 * K, L), L ** -0.5, 0.125, ((0, 64),))
    covariance = draw_covariance(jax.random.fold_in(jax.random.fold_in(streams_of[5], part), 71), part)
    noise_var = jnp.clip(jnp.exp(math.log(4.0) - 2.0794415 * jax.random.uniform(part_keys[2], (CHANNELS, K), jnp.float32) ** block_scale(part_keys[2], (CHANNELS, K), ((0, 64),), -0.2, 0.2)), 0.5, 4.0)
    start_field = scatter_about(part_keys[3], (CHANNELS, K, 2 * PROBE_VECTOR_COUNT), 0.5, 4.0, ((0, 64),), jnp.float32)
    probes = scatter_about(part_keys[4], (CHANNELS, K, 2 * PROBE_VECTOR_COUNT), 1.0, 6.0, ((0, 64),), jnp.float32)
    return dict(beam_table=beam_table, covariance=covariance, noise_var=noise_var, start_field=start_field, probes=probes)


WEIGHT = 0.2


def project_back(beam_table, field_b):
    def one_channel(pair):
        table, values = pair
        reals = values[:, :PROBE_VECTOR_COUNT]
        imags = values[:, PROBE_VECTOR_COUNT:]
        lower = jnp.concatenate([imags, -reals], axis=1)
        stacked = jnp.concatenate([values, lower], axis=0)
        return jnp.dot(table.T, stacked, preferred_element_type=jnp.float32)
    return lax.map(one_channel, (beam_table, field_b))


def project_out(beam_table, channel_mixed):
    def one_channel(pair):
        table, values = pair
        product = jnp.dot(table, values, preferred_element_type=jnp.float32)
        upper = product[:K]
        lower = product[K:]
        return jnp.concatenate([upper[:, :PROBE_VECTOR_COUNT] - lower[:, PROBE_VECTOR_COUNT:], upper[:, PROBE_VECTOR_COUNT:] + lower[:, :PROBE_VECTOR_COUNT]], axis=1)
    return lax.map(one_channel, (beam_table, channel_mixed))


def reference(beam_table, covariance, noise_var, start_field, probes):
    field = start_field
    covariance_broad = covariance.astype(jnp.float32)
    for repeat in range(ITERS):
        field_b = field.astype(jnp.bfloat16)
        sky_map = project_back(beam_table, field_b).astype(jnp.bfloat16)
        channel_mixed = jnp.einsum('drj,jdi->rdi', covariance_broad, sky_map.astype(jnp.float32)).astype(jnp.bfloat16)
        image = project_out(beam_table, channel_mixed)
        field = field + WEIGHT * (probes - image - noise_var[:, :, None] * field)
    final_sky = project_back(beam_table, field.astype(jnp.bfloat16)).astype(jnp.bfloat16)
    broad_sky_map = final_sky.astype(jnp.float32)
    multipole_band_power = (jnp.einsum('mjk,ujk->jmu', broad_sky_map, broad_sky_map) / PROBE_VECTOR_COUNT).astype(jnp.bfloat16)
    return field, multipole_band_power
```

```python
import jax
import jax.numpy as jnp
from jax import lax
from jax.sharding import PartitionSpec as P

ITERS = 2
WEIGHT = 0.2
CHUNKS = 2


def project_back(beam_table, field_b):
    column_entries = field_b.shape[2] // 2
    reals = field_b[:, :, :column_entries]
    imags = field_b[:, :, column_entries:]
    lower = jnp.concatenate([imags, -reals], axis=2)
    stacked = jnp.concatenate([field_b, lower], axis=1)
    return jnp.einsum("fkl,fkc->flc", beam_table, stacked, preferred_element_type=jnp.float32)


def project_out(beam_table, mixed_back):
    column_entries = mixed_back.shape[2] // 2
    modes = beam_table.shape[1] // 2
    product = jnp.einsum("fkl,flc->fkc", beam_table, mixed_back, preferred_element_type=jnp.float32)
    upper = product[:, :modes]
    lower = product[:, modes:]
    return jnp.concatenate(
        [
            upper[:, :, :column_entries] - lower[:, :, column_entries:],
            upper[:, :, column_entries:] + lower[:, :, :column_entries],
        ],
        axis=2,
    )


def apply_operator(beam_table, covariance, field):
    field_b = field.astype(jnp.bfloat16)
    sky_map = project_back(beam_table, field_b).astype(jnp.bfloat16)
    channel_mixed = jnp.einsum(
        "drj,jdi->rdi",
        covariance,
        lax.all_to_all(sky_map, "chan", split_axis=1, concat_axis=0, tiled=True),
        preferred_element_type=jnp.float32,
    )
    mixed_back = lax.all_to_all(
        channel_mixed.astype(jnp.bfloat16), "chan", split_axis=0, concat_axis=1, tiled=True
    )
    return project_out(beam_table, mixed_back)


def split_columns(x, chunks):
    half = x.shape[2] // 2
    width = half // chunks
    return [
        jnp.concatenate(
            [x[:, :, i * width:(i + 1) * width], x[:, :, half + i * width:half + (i + 1) * width]], axis=2
        )
        for i in range(chunks)
    ]


def join_columns(parts):
    width = parts[0].shape[2] // 2
    return jnp.concatenate([p[:, :, :width] for p in parts] + [p[:, :, width:] for p in parts], axis=2)


def on_device(beam_table, covariance, noise_var, start_field, probes):
    column_entries = start_field.shape[2] // 2
    fields = split_columns(start_field, CHUNKS)
    rhs = split_columns(probes, CHUNKS)
    noise = noise_var[:, :, None]
    for repeat in range(ITERS):
        for i in range(CHUNKS):
            image = apply_operator(beam_table, covariance, fields[i])
            fields[i] = fields[i] + WEIGHT * (rhs[i] - image - noise * fields[i])
    power = None
    for i in range(CHUNKS):
        final_sky = project_back(beam_table, fields[i].astype(jnp.bfloat16)).astype(jnp.bfloat16)
        collected = lax.all_to_all(final_sky, "chan", split_axis=1, concat_axis=0, tiled=True)
        part = jnp.einsum("mjk,ujk->jmu", collected, collected, preferred_element_type=jnp.float32)
        power = part if power is None else power + part
    multipole_band_power = power / column_entries
    return (join_columns(fields), multipole_band_power.astype(jnp.bfloat16))


def solution(mesh):
    return jax.shard_map(
        on_device,
        mesh=mesh,
        in_specs=(
            P(("ma", "chan"), None, None),
            P(("ma", "chan"), None, None),
            P(("ma", "chan"), None),
            P(("ma", "chan"), None, None),
            P(("ma", "chan"), None, None),
        ),
        out_specs=(P(("ma", "chan"), None, None), P(("ma", "chan"), None, None)),
        check_vma=False,
    )
```

```python
import functools

import jax
import jax.numpy as jnp
from jax import lax
from jax.experimental import pallas as pl
from jax.experimental.pallas import tpu as pltpu
from jax.sharding import PartitionSpec as P

ITERS = 2
WEIGHT = 0.2
L_BLOCK = 512


def stack_transposed(field):
    field_b = field.astype(jnp.bfloat16)
    half = field_b.shape[2] // 2
    reals = field_b[:, :, :half]
    imags = field_b[:, :, half:]
    lower = jnp.concatenate([imags, -reals], axis=2)
    stacked = jnp.concatenate([field_b, lower], axis=1)
    return jnp.swapaxes(stacked, 1, 2)


def _back_kernel(st_ref, b_ref, out_ref):
    acc = jnp.dot(st_ref[0], b_ref[0], preferred_element_type=jnp.float32)
    out_ref[...] = acc.T.astype(out_ref.dtype)


def project_back(beam_table, field):
    channels, rows, multipoles = beam_table.shape
    stacked_t = stack_transposed(field)
    columns = stacked_t.shape[1]
    blocks = multipoles // L_BLOCK
    return pl.pallas_call(
        _back_kernel,
        grid=(channels, blocks),
        in_specs=[
            pl.BlockSpec((1, columns, rows), lambda f, i: (f, 0, 0)),
            pl.BlockSpec((1, rows, L_BLOCK), lambda f, i: (f, 0, i)),
        ],
        out_specs=pl.BlockSpec((L_BLOCK, columns), lambda f, i: (i, f)),
        out_shape=jax.ShapeDtypeStruct((multipoles, channels * columns), jnp.bfloat16),
        cost_estimate=pl.CostEstimate(
            flops=2 * channels * rows * multipoles * columns,
            transcendentals=0,
            bytes_accessed=2 * (channels * rows * multipoles + channels * columns * rows + multipoles * channels * columns),
        ),
    )(stacked_t, beam_table)


def gather_sky(sky, devices):
    received = lax.all_to_all(sky, "chan", split_axis=0, concat_axis=0, tiled=True)
    local = received.shape[0] // devices
    split = received.reshape(devices, local, 2, received.shape[1] // 2)
    return jnp.transpose(split, (1, 0, 2, 3)).reshape(local, 2 * devices, received.shape[1] // 2)


def project_out(beam_table, mixed_back):
    column_entries = mixed_back.shape[2] // 2
    modes = beam_table.shape[1] // 2
    product = jnp.einsum("fkl,flc->fkc", beam_table, mixed_back, preferred_element_type=jnp.float32)
    upper = product[:, :modes]
    lower = product[:, modes:]
    return jnp.concatenate(
        [
            upper[:, :, :column_entries] - lower[:, :, column_entries:],
            upper[:, :, column_entries:] + lower[:, :, :column_entries],
        ],
        axis=2,
    )


def apply_operator(beam_table, covariance, field, devices):
    sky = gather_sky(project_back(beam_table, field), devices)
    channel_mixed = jnp.einsum("jpg,jgc->pjc", covariance, sky, preferred_element_type=jnp.float32)
    mixed_back = lax.all_to_all(
        channel_mixed.astype(jnp.bfloat16), "chan", split_axis=0, concat_axis=1, tiled=True
    )
    return project_out(beam_table, mixed_back)


def on_device(beam_table, covariance, noise_var, start_field, probes):
    devices = lax.axis_size("chan")
    column_entries = start_field.shape[2] // 2
    local, channels, _ = covariance.shape
    field = start_field
    for repeat in range(ITERS):
        image = apply_operator(beam_table, covariance, field, devices)
        field = field + WEIGHT * (probes - image - noise_var[:, :, None] * field)
    final_sky = gather_sky(project_back(beam_table, field), devices)
    power = jnp.einsum("jpc,jqc->jpq", final_sky, final_sky, preferred_element_type=jnp.float32) / column_entries
    return (field, power.astype(jnp.bfloat16))


def solution(mesh):
    return jax.shard_map(
        on_device,
        mesh=mesh,
        in_specs=(
            P(("ma", "chan"), None, None),
            P(("ma", "chan"), None, None),
            P(("ma", "chan"), None),
            P(("ma", "chan"), None, None),
            P(("ma", "chan"), None, None),
        ),
        out_specs=(P(("ma", "chan"), None, None), P(("ma", "chan"), None, None)),
        check_vma=False,
    )
```

```python
import functools

import jax
import jax.numpy as jnp
from jax import lax
from jax.experimental import pallas as pl
from jax.experimental.pallas import tpu as pltpu
from jax.sharding import PartitionSpec as P

ITERS = 2
WEIGHT = 0.2
ROW_BLOCK = 256


def _stack_t(new):
    half = new.shape[1] // 2
    t = new.astype(jnp.bfloat16).astype(jnp.float32).T
    zr_t = t[:half]
    zi_t = t[half:]
    top = jnp.concatenate([zr_t, zi_t], axis=1)
    bottom = jnp.concatenate([zi_t, -zr_t], axis=1)
    return jnp.concatenate([top, bottom], axis=0).astype(jnp.bfloat16)


def _sweep_kernel(with_update, *refs):
    if with_update:
        b_hbm, m_hbm, f_hbm, p_hbm, n_hbm, fld_out, sky_out, bv, mv, fv, pv, nv, sems = refs
    else:
        b_hbm, f_hbm, sky_out, bv, fv, sems = refs
    channels, rows, multipoles = bv.shape
    modes = fv.shape[1]
    blocks = modes // ROW_BLOCK
    slot = iter(range(sems.shape[0]))

    def start(src, dst):
        copy = pltpu.make_async_copy(src, dst, sems.at[next(slot)])
        copy.start()
        return copy

    small, beams = [], []
    for f in range(channels):
        group = [start(f_hbm.at[f], fv.at[f])]
        if with_update:
            group += [start(m_hbm.at[:, f], mv.at[f]), start(p_hbm.at[f], pv.at[f]), start(n_hbm.at[f], nv.at[f])]
        small.append(group)
        parts = []
        for kb in range(blocks):
            for base in (0, modes):
                lo = base + kb * ROW_BLOCK
                parts.append(start(b_hbm.at[f, pl.ds(lo, ROW_BLOCK)], bv.at[f, pl.ds(lo, ROW_BLOCK)]))
        beams.append(parts)

    for f in range(channels):
        for copy in small[f]:
            copy.wait()
        if with_update:
            m = mv[f].reshape(multipoles, mv.shape[3])
            half = fv.shape[2] // 2
            for kb in range(blocks):
                beams[f][2 * kb].wait()
                beams[f][2 * kb + 1].wait()
                upper = jnp.dot(bv[f, pl.ds(kb * ROW_BLOCK, ROW_BLOCK)], m, preferred_element_type=jnp.float32)
                lower = jnp.dot(bv[f, pl.ds(modes + kb * ROW_BLOCK, ROW_BLOCK)], m, preferred_element_type=jnp.float32)
                image = jnp.concatenate(
                    [upper[:, :half] - lower[:, half:], upper[:, half:] + lower[:, :half]], axis=1
                )
                fld = fv[f, pl.ds(kb * ROW_BLOCK, ROW_BLOCK)]
                rhs = pv[f, pl.ds(kb * ROW_BLOCK, ROW_BLOCK)]
                noise = nv[f, pl.ds(kb * ROW_BLOCK, ROW_BLOCK)]
                fld_out[f, pl.ds(kb * ROW_BLOCK, ROW_BLOCK)] = fld + WEIGHT * (rhs - image - noise * fld)
            new = fld_out[f]
        else:
            for copy in beams[f]:
                copy.wait()
            new = fv[f]
        sky = jnp.dot(_stack_t(new), bv[f], preferred_element_type=jnp.float32)
        sky_out[:, f, :] = sky.T.astype(sky_out.dtype)


def sweep(beam_table, field, mixed=None, probes=None, noise=None):
    channels, rows, multipoles = beam_table.shape
    modes, columns = field.shape[1], field.shape[2]
    with_update = mixed is not None
    any_space = pl.BlockSpec(memory_space=pl.ANY)
    vmem = pl.BlockSpec(memory_space=pltpu.MemorySpace.VMEM)
    sky_shape = jax.ShapeDtypeStruct((multipoles, channels, columns), jnp.bfloat16)
    blocks = modes // ROW_BLOCK
    flops = 2 * channels * rows * multipoles * columns
    scratch = [pltpu.VMEM(beam_table.shape, beam_table.dtype), pltpu.VMEM(field.shape, jnp.float32)]
    if with_update:
        devices = mixed.shape[0]
        scratch = [
            pltpu.VMEM(beam_table.shape, beam_table.dtype),
            pltpu.VMEM((channels, devices, mixed.shape[2], mixed.shape[3]), mixed.dtype),
            pltpu.VMEM(field.shape, jnp.float32),
            pltpu.VMEM(field.shape, jnp.float32),
            pltpu.VMEM((channels, modes, 1), jnp.float32),
        ]
        n_sems = channels * (4 + 2 * blocks)
        in_specs = [any_space] * 5
        out_specs = [vmem, vmem]
        out_shape = [jax.ShapeDtypeStruct(field.shape, jnp.float32), sky_shape]
        args = (beam_table, mixed, field, probes, noise[:, :, None])
        flops *= 2
    else:
        n_sems = channels * (1 + 2 * blocks)
        in_specs = [any_space] * 2
        out_specs = vmem
        out_shape = sky_shape
        args = (beam_table, field)
    return pl.pallas_call(
        functools.partial(_sweep_kernel, with_update),
        in_specs=in_specs,
        out_specs=out_specs,
        out_shape=out_shape,
        scratch_shapes=scratch + [pltpu.SemaphoreType.DMA((n_sems,))],
        compiler_params=pltpu.CompilerParams(vmem_limit_bytes=56 * 1024 * 1024),
        cost_estimate=pl.CostEstimate(
            flops=flops, transcendentals=0, bytes_accessed=2 * channels * rows * multipoles + 12 * 1024 * 1024
        ),
    )(*args)


def to_multipoles(sky):
    return lax.all_to_all(sky, "chan", split_axis=0, concat_axis=1, tiled=True)


def mix(covariance, sky):
    channel_mixed = jnp.einsum("drj,dji->rdi", covariance, sky, preferred_element_type=jnp.float32)
    back = lax.all_to_all(channel_mixed.astype(jnp.bfloat16), "chan", split_axis=0, concat_axis=0, tiled=True)
    channels = back.shape[0]
    return back.reshape(channels // 2, 2, back.shape[1], back.shape[2])


def on_device(beam_table, covariance, noise_var, start_field, probes):
    column_entries = start_field.shape[2] // 2
    field = start_field
    sky = sweep(beam_table, field)
    for repeat in range(ITERS):
        mixed = mix(covariance, to_multipoles(sky))
        field, sky = sweep(beam_table, field, mixed, probes, noise_var)
    collected = to_multipoles(sky)
    multipole_band_power = (
        jnp.einsum("jmk,juk->jmu", collected, collected, preferred_element_type=jnp.float32) / column_entries
    )
    return (field, multipole_band_power.astype(jnp.bfloat16))


def solution(mesh):
    return jax.shard_map(
        on_device,
        mesh=mesh,
        in_specs=(
            P(("ma", "chan"), None, None),
            P(("ma", "chan"), None, None),
            P(("ma", "chan"), None),
            P(("ma", "chan"), None, None),
            P(("ma", "chan"), None, None),
        ),
        out_specs=(P(("ma", "chan"), None, None), P(("ma", "chan"), None, None)),
        check_vma=False,
    )
```

```python
import functools

import jax
import jax.numpy as jnp
from jax import lax
from jax.experimental import pallas as pl
from jax.experimental.pallas import tpu as pltpu
from jax.sharding import PartitionSpec as P

ITERS = 2
WEIGHT = 0.2
ROW_BLOCK = 256
L_BLOCK = 512


def _stack_t(new):
    half = new.shape[1] // 2
    t = new.astype(jnp.bfloat16).astype(jnp.float32).T
    zr_t = t[:half]
    zi_t = t[half:]
    top = jnp.concatenate([zr_t, zi_t], axis=1)
    bottom = jnp.concatenate([zi_t, -zr_t], axis=1)
    return jnp.concatenate([top, bottom], axis=0).astype(jnp.bfloat16)


def _sweep_kernel(with_update, *refs):
    if with_update:
        b_hbm, m_hbm, f_hbm, p_hbm, n_hbm, fld_out, sky_out, bv, mv, fv, pv, nv, gv, sv, sems = refs
    else:
        b_hbm, f_hbm, sky_out, bv, fv, sv, sems = refs
    channels, rows, multipoles = bv.shape
    modes = fv.shape[1]
    blocks = modes // ROW_BLOCK
    slot = iter(range(sems.shape[0]))

    def start(src, dst):
        copy = pltpu.make_async_copy(src, dst, sems.at[next(slot)])
        copy.start()
        return copy

    small, beams, outgoing = [], [], []
    for f in range(channels):
        group = [start(f_hbm.at[f], fv.at[f])]
        if with_update:
            group += [start(m_hbm.at[:, f], mv.at[f]), start(p_hbm.at[f], pv.at[f]), start(n_hbm.at[f], nv.at[f])]
        small.append(group)
        parts = []
        for kb in range(blocks):
            for base in (0, modes):
                lo = base + kb * ROW_BLOCK
                parts.append(start(b_hbm.at[f, pl.ds(lo, ROW_BLOCK)], bv.at[f, pl.ds(lo, ROW_BLOCK)]))
        beams.append(parts)

    for f in range(channels):
        for copy in small[f]:
            copy.wait()
        if with_update:
            m = mv[f].reshape(multipoles, mv.shape[3])
            half = fv.shape[2] // 2
            for kb in range(blocks):
                beams[f][2 * kb].wait()
                beams[f][2 * kb + 1].wait()
                upper = jnp.dot(bv[f, pl.ds(kb * ROW_BLOCK, ROW_BLOCK)], m, preferred_element_type=jnp.float32)
                lower = jnp.dot(bv[f, pl.ds(modes + kb * ROW_BLOCK, ROW_BLOCK)], m, preferred_element_type=jnp.float32)
                image = jnp.concatenate(
                    [upper[:, :half] - lower[:, half:], upper[:, half:] + lower[:, :half]], axis=1
                )
                block = pl.ds(kb * ROW_BLOCK, ROW_BLOCK)
                fld = fv[f, block]
                gv[f, block] = fld + WEIGHT * (pv[f, block] - image - nv[f, block] * fld)
                outgoing.append(start(gv.at[f, block], fld_out.at[f, block]))
            stacked_t = _stack_t(gv[f])
        else:
            for copy in beams[f]:
                copy.wait()
            stacked_t = _stack_t(fv[f])
        for lb in range(multipoles // L_BLOCK):
            cols = pl.ds(lb * L_BLOCK, L_BLOCK)
            sky = jnp.dot(stacked_t, bv[f, :, cols], preferred_element_type=jnp.float32)
            sv[cols, f, :] = sky.T.astype(sv.dtype)
            if f == channels - 1:
                outgoing.append(start(sv.at[cols], sky_out.at[cols]))
    for copy in outgoing:
        copy.wait()


def sweep(beam_table, field, mixed=None, probes=None, noise=None):
    channels, rows, multipoles = beam_table.shape
    modes, columns = field.shape[1], field.shape[2]
    with_update = mixed is not None
    any_space = pl.BlockSpec(memory_space=pl.ANY)
    sky_shape = jax.ShapeDtypeStruct((multipoles, channels, columns), jnp.bfloat16)
    blocks = modes // ROW_BLOCK
    flops = 2 * channels * rows * multipoles * columns
    sky_scratch = pltpu.VMEM((multipoles, channels, columns), jnp.bfloat16)
    scratch = [pltpu.VMEM(beam_table.shape, beam_table.dtype), pltpu.VMEM(field.shape, jnp.float32), sky_scratch]
    if with_update:
        devices = mixed.shape[0]
        scratch = [
            pltpu.VMEM(beam_table.shape, beam_table.dtype),
            pltpu.VMEM((channels, devices, mixed.shape[2], mixed.shape[3]), mixed.dtype),
            pltpu.VMEM(field.shape, jnp.float32),
            pltpu.VMEM(field.shape, jnp.float32),
            pltpu.VMEM((channels, modes, 1), jnp.float32),
            pltpu.VMEM(field.shape, jnp.float32),
            sky_scratch,
        ]
        n_sems = channels * (4 + 3 * blocks) + multipoles // L_BLOCK
        in_specs = [any_space] * 5
        out_specs = [any_space, any_space]
        out_shape = [jax.ShapeDtypeStruct(field.shape, jnp.float32), sky_shape]
        args = (beam_table, mixed, field, probes, noise[:, :, None])
        flops *= 2
    else:
        n_sems = channels * (1 + 2 * blocks) + multipoles // L_BLOCK
        in_specs = [any_space] * 2
        out_specs = any_space
        out_shape = sky_shape
        args = (beam_table, field)
    return pl.pallas_call(
        functools.partial(_sweep_kernel, with_update),
        in_specs=in_specs,
        out_specs=out_specs,
        out_shape=out_shape,
        scratch_shapes=scratch + [pltpu.SemaphoreType.DMA((n_sems,))],
        compiler_params=pltpu.CompilerParams(vmem_limit_bytes=56 * 1024 * 1024),
        cost_estimate=pl.CostEstimate(
            flops=flops, transcendentals=0, bytes_accessed=2 * channels * rows * multipoles + 12 * 1024 * 1024
        ),
    )(*args)


def to_multipoles(sky):
    return lax.all_to_all(sky, "chan", split_axis=0, concat_axis=1, tiled=True)


def mix(covariance, sky):
    channel_mixed = jnp.einsum("drj,dji->rdi", covariance, sky, preferred_element_type=jnp.float32)
    back = lax.all_to_all(channel_mixed.astype(jnp.bfloat16), "chan", split_axis=0, concat_axis=0, tiled=True)
    channels = back.shape[0]
    return back.reshape(channels // 2, 2, back.shape[1], back.shape[2])


def on_device(beam_table, covariance, noise_var, start_field, probes):
    column_entries = start_field.shape[2] // 2
    field = start_field
    sky = sweep(beam_table, field)
    for repeat in range(ITERS):
        mixed = mix(covariance, to_multipoles(sky))
        field, sky = sweep(beam_table, field, mixed, probes, noise_var)
    collected = to_multipoles(sky)
    multipole_band_power = (
        jnp.einsum("jmk,juk->jmu", collected, collected, preferred_element_type=jnp.float32) / column_entries
    )
    return (field, multipole_band_power.astype(jnp.bfloat16))


def solution(mesh):
    return jax.shard_map(
        on_device,
        mesh=mesh,
        in_specs=(
            P(("ma", "chan"), None, None),
            P(("ma", "chan"), None, None),
            P(("ma", "chan"), None),
            P(("ma", "chan"), None, None),
            P(("ma", "chan"), None, None),
        ),
        out_specs=(P(("ma", "chan"), None, None), P(("ma", "chan"), None, None)),
        check_vma=False,
    )
```

```python
import functools

import jax
import jax.numpy as jnp
from jax import lax
from jax.experimental import pallas as pl
from jax.experimental.pallas import tpu as pltpu
from jax.sharding import PartitionSpec as P

ITERS = 2
WEIGHT = 0.2
ROW_BLOCK = 256
L_BLOCK = 512


def _stack_t(new):
    half = new.shape[1] // 2
    t = new.astype(jnp.bfloat16).astype(jnp.float32).T
    zr_t = t[:half]
    zi_t = t[half:]
    top = jnp.concatenate([zr_t, zi_t], axis=1)
    bottom = jnp.concatenate([zi_t, -zr_t], axis=1)
    return jnp.concatenate([top, bottom], axis=0).astype(jnp.bfloat16)


def _sweep_kernel(with_update, *refs):
    if with_update:
        b_hbm, m_hbm, f_hbm, p_hbm, n_hbm, fld_out, sky_out, bv, mv, fv, pv, gv, sv, sems = refs
    else:
        b_hbm, f_hbm, sky_out, bv, fv, sv, sems = refs
    channels, rows, multipoles = bv.shape
    modes = fv.shape[1]
    blocks = modes // ROW_BLOCK
    slot = iter(range(sems.shape[0]))

    def start(src, dst):
        copy = pltpu.make_async_copy(src, dst, sems.at[next(slot)])
        copy.start()
        return copy

    small, beams, outgoing = [], [], []
    for f in range(channels):
        group = [start(f_hbm.at[f], fv.at[f])]
        if with_update:
            group += [start(m_hbm.at[:, f], mv.at[f]), start(p_hbm.at[f], pv.at[f])]
        small.append(group)
        parts = []
        for kb in range(blocks):
            for base in (0, modes):
                lo = base + kb * ROW_BLOCK
                parts.append(start(b_hbm.at[f, pl.ds(lo, ROW_BLOCK)], bv.at[f, pl.ds(lo, ROW_BLOCK)]))
        beams.append(parts)

    for f in range(channels):
        for copy in small[f]:
            copy.wait()
        if with_update:
            m = mv[f].reshape(multipoles, mv.shape[3])
            noise_row = n_hbm[pl.ds(f, 1), :]
            noise_col = jnp.broadcast_to(noise_row, (128, modes)).T[:, :1]
            half = fv.shape[2] // 2
            for kb in range(blocks):
                beams[f][2 * kb].wait()
                beams[f][2 * kb + 1].wait()
                upper = jnp.dot(bv[f, pl.ds(kb * ROW_BLOCK, ROW_BLOCK)], m, preferred_element_type=jnp.float32)
                lower = jnp.dot(bv[f, pl.ds(modes + kb * ROW_BLOCK, ROW_BLOCK)], m, preferred_element_type=jnp.float32)
                image = jnp.concatenate(
                    [upper[:, :half] - lower[:, half:], upper[:, half:] + lower[:, :half]], axis=1
                )
                block = pl.ds(kb * ROW_BLOCK, ROW_BLOCK)
                fld = fv[f, block]
                gv[f, block] = fld + WEIGHT * (pv[f, block] - image - noise_col[kb * ROW_BLOCK:(kb + 1) * ROW_BLOCK] * fld)
                outgoing.append(start(gv.at[f, block], fld_out.at[f, block]))
            stacked_t = _stack_t(gv[f])
        else:
            for copy in beams[f]:
                copy.wait()
            stacked_t = _stack_t(fv[f])
        for lb in range(multipoles // L_BLOCK):
            cols = pl.ds(lb * L_BLOCK, L_BLOCK)
            sky = jnp.dot(stacked_t, bv[f, :, cols], preferred_element_type=jnp.float32)
            sv[cols, f, :] = sky.T.astype(sv.dtype)
            if f == channels - 1:
                outgoing.append(start(sv.at[cols], sky_out.at[cols]))
    for copy in outgoing:
        copy.wait()


def sweep(beam_table, field, mixed=None, probes=None, noise=None):
    channels, rows, multipoles = beam_table.shape
    modes, columns = field.shape[1], field.shape[2]
    with_update = mixed is not None
    any_space = pl.BlockSpec(memory_space=pl.ANY)
    sky_shape = jax.ShapeDtypeStruct((multipoles, channels, columns), jnp.bfloat16)
    blocks = modes // ROW_BLOCK
    flops = 2 * channels * rows * multipoles * columns
    sky_scratch = pltpu.VMEM((multipoles, channels, columns), jnp.bfloat16)
    scratch = [pltpu.VMEM(beam_table.shape, beam_table.dtype), pltpu.VMEM(field.shape, jnp.float32), sky_scratch]
    if with_update:
        devices = mixed.shape[0]
        scratch = [
            pltpu.VMEM(beam_table.shape, beam_table.dtype),
            pltpu.VMEM((channels, devices, mixed.shape[2], mixed.shape[3]), mixed.dtype),
            pltpu.VMEM(field.shape, jnp.float32),
            pltpu.VMEM(field.shape, jnp.float32),
            pltpu.VMEM(field.shape, jnp.float32),
            sky_scratch,
        ]
        n_sems = channels * (3 + 3 * blocks) + multipoles // L_BLOCK
        in_specs = [any_space] * 4 + [pl.BlockSpec(memory_space=pltpu.MemorySpace.VMEM)]
        out_specs = [any_space, any_space]
        out_shape = [jax.ShapeDtypeStruct(field.shape, jnp.float32), sky_shape]
        args = (beam_table, mixed, field, probes, noise)
        flops *= 2
    else:
        n_sems = channels * (1 + 2 * blocks) + multipoles // L_BLOCK
        in_specs = [any_space] * 2
        out_specs = any_space
        out_shape = sky_shape
        args = (beam_table, field)
    return pl.pallas_call(
        functools.partial(_sweep_kernel, with_update),
        in_specs=in_specs,
        out_specs=out_specs,
        out_shape=out_shape,
        scratch_shapes=scratch + [pltpu.SemaphoreType.DMA((n_sems,))],
        compiler_params=pltpu.CompilerParams(vmem_limit_bytes=56 * 1024 * 1024),
        cost_estimate=pl.CostEstimate(
            flops=flops, transcendentals=0, bytes_accessed=2 * channels * rows * multipoles + 12 * 1024 * 1024
        ),
    )(*args)


def to_multipoles(sky):
    return lax.all_to_all(sky, "chan", split_axis=0, concat_axis=1, tiled=True)


def mix(covariance, sky):
    channel_mixed = jnp.einsum("drj,dji->rdi", covariance, sky, preferred_element_type=jnp.float32)
    back = lax.all_to_all(channel_mixed.astype(jnp.bfloat16), "chan", split_axis=0, concat_axis=0, tiled=True)
    channels = back.shape[0]
    return back.reshape(channels // 2, 2, back.shape[1], back.shape[2])


def on_device(beam_table, covariance, noise_var, start_field, probes):
    column_entries = start_field.shape[2] // 2
    field = start_field
    sky = sweep(beam_table, field)
    for repeat in range(ITERS):
        mixed = mix(covariance, to_multipoles(sky))
        field, sky = sweep(beam_table, field, mixed, probes, noise_var)
    collected = to_multipoles(sky)
    multipole_band_power = (
        jnp.einsum("jmk,juk->jmu", collected, collected, preferred_element_type=jnp.float32) / column_entries
    )
    return (field, multipole_band_power.astype(jnp.bfloat16))


def solution(mesh):
    return jax.shard_map(
        on_device,
        mesh=mesh,
        in_specs=(
            P(("ma", "chan"), None, None),
            P(("ma", "chan"), None, None),
            P(("ma", "chan"), None),
            P(("ma", "chan"), None, None),
            P(("ma", "chan"), None, None),
        ),
        out_specs=(P(("ma", "chan"), None, None), P(("ma", "chan"), None, None)),
        check_vma=False,
    )
```

```python
import functools

import jax
import jax.numpy as jnp
from jax import lax
from jax.experimental import pallas as pl
from jax.experimental.pallas import tpu as pltpu
from jax.sharding import PartitionSpec as P

ITERS = 2
WEIGHT = 0.2
ROW_BLOCK = 256
L_BLOCK = 512


def _stack_t(new):
    half = new.shape[1] // 2
    t = new.astype(jnp.bfloat16).astype(jnp.float32).T
    zr_t = t[:half]
    zi_t = t[half:]
    top = jnp.concatenate([zr_t, zi_t], axis=1)
    bottom = jnp.concatenate([zi_t, -zr_t], axis=1)
    return jnp.concatenate([top, bottom], axis=0).astype(jnp.bfloat16)


def _sweep_kernel(with_update, *refs):
    if with_update:
        b_hbm, m_hbm, f_hbm, p_hbm, n_hbm, fld_out, sky_out, bv, mv, fv, pv, nv, gv, sv, sems = refs
    else:
        b_hbm, f_hbm, sky_out, bv, fv, sv, sems = refs
    channels, rows, multipoles = bv.shape
    modes = fv.shape[1]
    blocks = modes // ROW_BLOCK
    slot = iter(range(sems.shape[0]))

    def start(src, dst):
        copy = pltpu.make_async_copy(src, dst, sems.at[next(slot)])
        copy.start()
        return copy

    small, beams, outgoing = [], [], []
    for f in range(channels):
        group = [start(f_hbm.at[f], fv.at[f])]
        if with_update:
            group += [start(m_hbm.at[:, f], mv.at[f]), start(p_hbm.at[f], pv.at[f])]
            if f == 0:
                group.append(start(n_hbm, nv))
        small.append(group)
        parts = []
        for kb in range(blocks):
            for base in (0, modes):
                lo = base + kb * ROW_BLOCK
                parts.append(start(b_hbm.at[f, pl.ds(lo, ROW_BLOCK)], bv.at[f, pl.ds(lo, ROW_BLOCK)]))
        beams.append(parts)

    for f in range(channels):
        for copy in small[f]:
            copy.wait()
        if with_update:
            m = mv[f].reshape(multipoles, mv.shape[3])
            noise_row = nv[pl.ds(f, 1), :]
            noise_col = jnp.broadcast_to(noise_row, (128, modes)).T[:, :1]
            half = fv.shape[2] // 2
            for kb in range(blocks):
                beams[f][2 * kb].wait()
                beams[f][2 * kb + 1].wait()
                upper = jnp.dot(bv[f, pl.ds(kb * ROW_BLOCK, ROW_BLOCK)], m, preferred_element_type=jnp.float32)
                lower = jnp.dot(bv[f, pl.ds(modes + kb * ROW_BLOCK, ROW_BLOCK)], m, preferred_element_type=jnp.float32)
                image = jnp.concatenate(
                    [upper[:, :half] - lower[:, half:], upper[:, half:] + lower[:, :half]], axis=1
                )
                block = pl.ds(kb * ROW_BLOCK, ROW_BLOCK)
                fld = fv[f, block]
                gv[f, block] = fld + WEIGHT * (pv[f, block] - image - noise_col[kb * ROW_BLOCK:(kb + 1) * ROW_BLOCK] * fld)
                outgoing.append(start(gv.at[f, block], fld_out.at[f, block]))
            stacked_t = _stack_t(gv[f])
        else:
            for copy in beams[f]:
                copy.wait()
            stacked_t = _stack_t(fv[f])
        for lb in range(multipoles // L_BLOCK):
            cols = pl.ds(lb * L_BLOCK, L_BLOCK)
            sky = jnp.dot(stacked_t, bv[f, :, cols], preferred_element_type=jnp.float32)
            sv[cols, f, :] = sky.T.astype(sv.dtype)
            if f == channels - 1:
                outgoing.append(start(sv.at[cols], sky_out.at[cols]))
    for copy in outgoing:
        copy.wait()


def sweep(beam_table, field, mixed=None, probes=None, noise=None):
    channels, rows, multipoles = beam_table.shape
    modes, columns = field.shape[1], field.shape[2]
    with_update = mixed is not None
    any_space = pl.BlockSpec(memory_space=pl.ANY)
    sky_shape = jax.ShapeDtypeStruct((multipoles, channels, columns), jnp.bfloat16)
    blocks = modes // ROW_BLOCK
    flops = 2 * channels * rows * multipoles * columns
    sky_scratch = pltpu.VMEM((multipoles, channels, columns), jnp.bfloat16)
    scratch = [pltpu.VMEM(beam_table.shape, beam_table.dtype), pltpu.VMEM(field.shape, jnp.float32), sky_scratch]
    if with_update:
        devices = mixed.shape[0]
        scratch = [
            pltpu.VMEM(beam_table.shape, beam_table.dtype),
            pltpu.VMEM((channels, devices, mixed.shape[2], mixed.shape[3]), mixed.dtype),
            pltpu.VMEM(field.shape, jnp.float32),
            pltpu.VMEM(field.shape, jnp.float32),
            pltpu.VMEM(noise.shape, jnp.float32),
            pltpu.VMEM(field.shape, jnp.float32),
            sky_scratch,
        ]
        n_sems = channels * (3 + 3 * blocks) + 1 + multipoles // L_BLOCK
        in_specs = [any_space] * 5
        out_specs = [any_space, any_space]
        out_shape = [jax.ShapeDtypeStruct(field.shape, jnp.float32), sky_shape]
        args = (beam_table, mixed, field, probes, noise)
        flops *= 2
    else:
        n_sems = channels * (1 + 2 * blocks) + multipoles // L_BLOCK
        in_specs = [any_space] * 2
        out_specs = any_space
        out_shape = sky_shape
        args = (beam_table, field)
    return pl.pallas_call(
        functools.partial(_sweep_kernel, with_update),
        in_specs=in_specs,
        out_specs=out_specs,
        out_shape=out_shape,
        scratch_shapes=scratch + [pltpu.SemaphoreType.DMA((n_sems,))],
        compiler_params=pltpu.CompilerParams(vmem_limit_bytes=56 * 1024 * 1024),
        cost_estimate=pl.CostEstimate(
            flops=flops, transcendentals=0, bytes_accessed=2 * channels * rows * multipoles + 12 * 1024 * 1024
        ),
    )(*args)


def to_multipoles(sky):
    return lax.all_to_all(sky, "chan", split_axis=0, concat_axis=1, tiled=True)


def mix(covariance, sky):
    channel_mixed = jnp.einsum("drj,dji->rdi", covariance, sky, preferred_element_type=jnp.float32)
    back = lax.all_to_all(channel_mixed.astype(jnp.bfloat16), "chan", split_axis=0, concat_axis=0, tiled=True)
    channels = back.shape[0]
    return back.reshape(channels // 2, 2, back.shape[1], back.shape[2])


def on_device(beam_table, covariance, noise_var, start_field, probes):
    column_entries = start_field.shape[2] // 2
    field = start_field
    sky = sweep(beam_table, field)
    for repeat in range(ITERS):
        mixed = mix(covariance, to_multipoles(sky))
        field, sky = sweep(beam_table, field, mixed, probes, noise_var)
    collected = to_multipoles(sky)
    multipole_band_power = (
        jnp.einsum("jmk,juk->jmu", collected, collected, preferred_element_type=jnp.float32) / column_entries
    )
    return (field, multipole_band_power.astype(jnp.bfloat16))


def solution(mesh):
    return jax.shard_map(
        on_device,
        mesh=mesh,
        in_specs=(
            P(("ma", "chan"), None, None),
            P(("ma", "chan"), None, None),
            P(("ma", "chan"), None),
            P(("ma", "chan"), None, None),
            P(("ma", "chan"), None, None),
        ),
        out_specs=(P(("ma", "chan"), None, None), P(("ma", "chan"), None, None)),
        check_vma=False,
    )
```
